256 devices in a mesh: dp: 128 (over x, y, z_hi, core), rep: 2 (over z_lo).
Axes of the slice: x: 4, y: 4, z: 8 (z_hi: 4, z_lo: 2; z = z_hi * 2 + z_lo), core: 2. Of those that a mesh axis runs over, the one named last changes fastest.
Arguments:
- queries: bfloat16 [262144, 1024], P(('dp', 'rep')), may hold values from -12 to 12
- keys: bfloat16 [16384, 1024], P('dp'), may hold values from -5 to 5
- neg_mask: int32 [2048, 128], P(('dp', 'rep')), may hold values from 0 to 1, as said below
- positive: int32 [2048], P(('dp', 'rep')), may hold values from 0 to 127, as said below
- row_weight: float32 [262144], P(('dp', 'rep')), may hold values from 2 to 20
Outputs:
- row_loss: float32 [262144], P(('dp', 'rep'))
- grad_queries: float32 [262144, 1024], P(('dp', 'rep'))
- grad_keys: float32 [16384, 1024], P(('dp', 'rep'))
The draws below stay inside these ranges and needn't reach their ends.
Inputs may be any that keep to these rules, and one draw needn't show every extreme that they name: neg_mask[b, c] is 0 unless key block c lies at cyclic distance at most 4 from the dp index that holds query block b (query blocks numbered along dp+rep, 8 to a device); for every b the two key blocks at distance exactly 4 are 1. positive[b] lies at cyclic distance at most 4 from the dp index that holds query block b.
All inputs are finite; a program needn't handle non-finite values.
Results may differ from the reference program's by a relative error of at most 0.003.
Values may be sent and summed in bfloat16 or wider, within the bound.
No kernel may reach another device: no remote copies, remote signals or barrier semaphores. Data moves between devices by JAX's collectives and lax.ppermute only.
A program may use at most 128 MiB of HBM per device.

```python
import math
import jax
import jax.numpy as jnp
from jax import lax

D = 1024
BLOCK = 128
REACH = 4
QB_DEV = 8
NQB = 2048
NKB = 128
NQ = 262144
NK = 16384
N_DP = 128
N_REP = 2


def positive_blocks(key):
    block_ids = jnp.arange(NQB, dtype=jnp.int32)
    home_idx = block_ids // (QB_DEV * N_REP)
    offset_draw = jax.random.randint(jax.random.fold_in(key, 7), (NQB,), -REACH, REACH + 1, dtype=jnp.int32)
    target = (home_idx + offset_draw) % N_DP
    target = jnp.where(block_ids == 0, N_DP - 1, target)
    target = jnp.where(block_ids == NQB - 1, 0, target)
    return target.astype(jnp.int32)


def key_table(key):
    key_base = jax.random.fold_in(key, 11)
    return jnp.clip(jax.random.normal(key_base, (NK, D), jnp.float32), -4.5, 4.5)


def draw_keys(key, part):
    return key_table(key).astype(jnp.bfloat16)


def draw_positive(key, part):
    return positive_blocks(key)


def draw_queries(key, part):
    table = key_table(key)
    target = positive_blocks(key)
    row_ids = jnp.arange(NQ, dtype=jnp.int32)
    block_ids = row_ids // BLOCK
    key_rows = target[block_ids] * BLOCK + row_ids % BLOCK
    positive_keys = table[key_rows]
    noise_key = jax.random.fold_in(key, 17)
    noise_part = jnp.clip(jax.random.normal(noise_key, (NQ, D), jnp.float32), -4.5, 4.5)
    mixed = 0.1 * positive_keys + noise_part
    return mixed.astype(jnp.bfloat16)


def draw_neg_mask(key, part):
    key_one = jax.random.fold_in(key, 13)
    key_two = jax.random.fold_in(key, 23)
    block_ids = jnp.arange(NQB, dtype=jnp.int32)
    home_idx = block_ids // (QB_DEV * N_REP)
    key_blocks = jnp.arange(NKB, dtype=jnp.int32)
    distance = (key_blocks[None, :] - home_idx[:, None]) % N_DP
    nearby = (distance <= REACH) | (distance >= N_DP - REACH)
    density = jax.random.randint(key_one, (NQB, 1), 1, 9, dtype=jnp.int32)
    coin_draw = jax.random.randint(key_two, (NQB, NKB), 0, 8, dtype=jnp.int32)
    chosen = nearby & (coin_draw < density)
    boundary = (distance == REACH) | (distance == N_DP - REACH)
    return jnp.where(chosen | boundary, 1, 0).astype(jnp.int32)


def block_scale(own_key, shape, split, low, largest):
    def one(dim, shards_of):
        draws = jax.random.uniform(jax.random.fold_in(jax.random.fold_in(own_key, 6), dim), (shards_of,), jnp.float32, low / len(split), largest / len(split))
        return jnp.repeat(jnp.exp(draws), shape[dim] // shards_of).reshape((-1,) + (1,) * (len(shape) - dim - 1))

    factor_of = one(*split[0])
    for cut in split[1:]:
        factor_of = factor_of * one(*cut)
    return factor_of


def setup_inputs(seed: int = 0) -> dict:
    splits = jax.random.split(jax.random.key(seed), 6)
    return {
        "queries": draw_queries(jax.random.fold_in(splits[5], 71), 0),
        "keys": draw_keys(jax.random.fold_in(splits[5], 71), 0),
        "neg_mask": draw_neg_mask(jax.random.fold_in(splits[5], 71), 0),
        "positive": draw_positive(jax.random.fold_in(splits[5], 71), 0),
        "row_weight": jnp.clip(jnp.exp(math.log(20.0) - 2.3025851 * jax.random.uniform(splits[4], (NQ,), jnp.float32) ** block_scale(splits[4], (NQ,), ((0, 256),), -0.2, 0.2)), 2.0, 20.0),
    }


def reference(queries, keys, neg_mask, positive, row_weight):
    logit_scale = 2.0 / math.sqrt(D)
    block_count = N_REP * QB_DEV
    group_rows = block_count * BLOCK
    window_len = 2 * REACH + 1
    offsets = jnp.arange(-REACH, REACH + 1, dtype=jnp.int32)
    inner_idx = jnp.arange(BLOCK, dtype=jnp.int32)
    same_row = inner_idx[:, None] == inner_idx[None, :]

    def one_shard(grad_keys, home_idx):
        first_block = (home_idx * block_count).astype(jnp.int32)
        first_row = (first_block * BLOCK).astype(jnp.int32)
        query_rows = lax.dynamic_slice_in_dim(queries, first_row, group_rows, 0)
        weights = lax.dynamic_slice_in_dim(row_weight, first_row, group_rows, 0)
        blocks = lax.dynamic_slice_in_dim(neg_mask, first_block, block_count, 0)
        pos_blocks = lax.dynamic_slice_in_dim(positive, first_block, block_count, 0)
        window = ((home_idx + offsets) % N_DP).astype(jnp.int32)
        key_rows = (window[:, None] * BLOCK + inner_idx[None, :]).reshape(window_len * BLOCK).astype(jnp.int32)
        window_keys = jnp.take(keys, key_rows, axis=0)
        logits = logit_scale * jnp.dot(query_rows, window_keys.T, preferred_element_type=jnp.float32)
        hit_block = pos_blocks[:, None] == window[None, :]
        allow_block = (jnp.take(blocks, window, axis=1) == 1) | hit_block
        allowed = jnp.broadcast_to(allow_block[:, None, :, None], (block_count, BLOCK, window_len, BLOCK)).reshape(group_rows, window_len * BLOCK)
        at_positive = (hit_block[:, None, :, None] & same_row[None, :, None, :]).reshape(group_rows, window_len * BLOCK)
        masked = jnp.where(allowed, logits, jnp.float32(-1e+30))
        row_max = lax.optimization_barrier(jnp.max(masked, axis=1, keepdims=True))
        row_sum = lax.optimization_barrier(jnp.sum(jnp.exp(masked - row_max), axis=1, keepdims=True))
        log_total = row_max + jnp.log(row_sum)
        pos_logit = lax.optimization_barrier(jnp.sum(jnp.where(at_positive, logits, jnp.float32(0.0)), axis=1))
        row_losses = log_total[:, 0] - pos_logit
        softmax_p = jnp.exp(masked - log_total)
        coefficient = (weights[:, None] * (softmax_p - at_positive.astype(jnp.float32))).astype(jnp.bfloat16)
        grad_query = logit_scale * jnp.dot(coefficient, window_keys, preferred_element_type=jnp.float32)
        grad_part = logit_scale * jnp.dot(coefficient.T, query_rows, preferred_element_type=jnp.float32)
        grad_keys = grad_keys.at[key_rows].add(grad_part)
        return (grad_keys, (row_losses, grad_query))
    grad_keys, outputs = lax.scan(one_shard, jnp.zeros((NK, D), jnp.float32), jnp.arange(N_DP, dtype=jnp.int32))
    row_losses, grad_query = outputs
    return (row_losses.reshape(NQ), grad_query.reshape(NQ, D), grad_keys)
```

```python
import math

import jax
import jax.numpy as jnp
from jax import lax
from jax.sharding import PartitionSpec as P

D = 1024
REACH = 4


def passed_along(x, axis, by):
    count = lax.axis_size(axis)
    return lax.ppermute(x, axis, [(i, (i + by) % count) for i in range(count)])


def swapped(x, axis):
    count = lax.axis_size(axis)
    return lax.ppermute(x, axis, [(i, i ^ 1) for i in range(count)])


def body(queries, keys, neg_mask, positive, row_weight):
    logit_scale = 2.0 / math.sqrt(D)
    cycle_size = lax.axis_size("dp")
    cycle_index = lax.axis_index("dp")
    rep_index = lax.axis_index("rep")
    core = cycle_index % 2
    delta = 1 - 2 * core
    query_rows = queries.shape[0]
    tile_rows = keys.shape[0]
    query_blocks = query_rows // tile_rows
    inner_idx = jnp.arange(tile_rows, dtype=jnp.int32)
    same_row = inner_idx[:, None] == inner_idx[None, :]

    down2 = passed_along(keys, "dp", 2)
    up2 = passed_along(keys, "dp", -2)
    down4 = passed_along(down2, "dp", 2)
    up4 = passed_along(up2, "dp", -2)
    sw_own = swapped(keys, "dp")
    sw_down2 = swapped(down2, "dp")
    sw_up2 = swapped(up2, "dp")
    sw_far = swapped(jnp.where(core == 0, up4, down4), "dp")
    key_tiles = [
        ("own", keys, 0),
        ("sw_own", sw_own, delta),
        ("down2", down2, -2),
        ("up2", up2, 2),
        ("sw_down2", sw_down2, delta - 2),
        ("sw_up2", sw_up2, delta + 2),
        ("down4", down4, -4),
        ("up4", up4, 4),
        ("sw_far", sw_far, -3 * delta),
    ]
    run_max = jnp.full((query_rows,), -1e30, jnp.float32)
    run_sum = jnp.zeros((query_rows,), jnp.float32)
    pos_logit = jnp.zeros((query_rows,), jnp.float32)
    stored = []
    for name, key_tile, offset in key_tiles:
        owner_idx = (cycle_index + offset) % cycle_size
        column = lax.dynamic_slice_in_dim(neg_mask, owner_idx, 1, 1)[:, 0]
        hit_block = positive == owner_idx
        allow_block = (column == 1) | hit_block
        allowed = jnp.broadcast_to(
            allow_block[:, None, None], (query_blocks, tile_rows, tile_rows)
        ).reshape(query_rows, tile_rows)
        at_positive = (hit_block[:, None, None] & same_row[None, :, :]).reshape(
            query_rows, tile_rows
        )
        logit_tile = logit_scale * lax.dot_general(
            queries, key_tile, (((1,), (1,)), ((), ())), preferred_element_type=jnp.float32
        )
        masked = jnp.where(allowed, logit_tile, jnp.float32(-1e30))
        next_max = jnp.maximum(run_max, jnp.max(masked, axis=1))
        run_sum = run_sum * jnp.exp(run_max - next_max) + jnp.sum(
            jnp.where(allowed, jnp.exp(masked - next_max[:, None]), 0.0), axis=1
        )
        run_max = next_max
        pos_logit = pos_logit + jnp.sum(jnp.where(at_positive, logit_tile, 0.0), axis=1)
        stored.append((name, key_tile, masked, at_positive))
    log_total = run_max + jnp.log(run_sum)
    row_loss = log_total - pos_logit
    grad_query = jnp.zeros(queries.shape, jnp.float32)
    key_parts = {}
    for name, key_tile, masked, at_positive in stored:
        softmax_p = jnp.exp(masked - log_total[:, None])
        coefficient = (row_weight[:, None] * (softmax_p - at_positive.astype(jnp.float32))).astype(
            jnp.bfloat16
        )
        grad_query = grad_query + logit_scale * jnp.dot(
            coefficient, key_tile, preferred_element_type=jnp.float32
        )
        key_parts[name] = lax.dot_general(
            coefficient, queries, (((0,), (0,)), ((), ())), preferred_element_type=jnp.float32
        )
    back_own = swapped(key_parts["sw_own"], "dp")
    back_down2 = swapped(key_parts["sw_down2"], "dp")
    back_up2 = swapped(key_parts["sw_up2"], "dp")
    back_far = swapped(key_parts["sw_far"], "dp")
    zero = jnp.zeros_like(back_far)
    far_up = key_parts["up4"] + jnp.where(core == 0, back_far, zero)
    far_down = key_parts["down4"] + jnp.where(core == 0, zero, back_far)
    near_up = key_parts["up2"] + back_up2 + passed_along(far_up, "dp", 2)
    near_down = key_parts["down2"] + back_down2 + passed_along(far_down, "dp", -2)
    total = (
        key_parts["own"]
        + back_own
        + passed_along(near_up, "dp", 2)
        + passed_along(near_down, "dp", -2)
    )
    half = tile_rows // 2
    halves = total.reshape(2, half, total.shape[1])
    mine = jnp.where(rep_index == 0, halves[0], halves[1])
    other = jnp.where(rep_index == 0, halves[1], halves[0])
    grad_keys = logit_scale * (mine + lax.ppermute(other, "rep", [(0, 1), (1, 0)]))
    return (row_loss, grad_query, grad_keys)


def solution(mesh):
    placed = (
        P(("dp", "rep"), None),
        P("dp", None),
        P(("dp", "rep"), None),
        P(("dp", "rep")),
        P(("dp", "rep")),
    )
    return jax.shard_map(
        body,
        mesh=mesh,
        in_specs=placed,
        out_specs=(P(("dp", "rep")), P(("dp", "rep"), None), P(("dp", "rep"), None)),
        check_vma=False,
    )
```

```python
import math

import jax
import jax.numpy as jnp
from jax import lax
from jax.sharding import PartitionSpec as P

D = 1024
REACH = 4


def passed_along(x, axis, by):
    count = lax.axis_size(axis)
    return lax.ppermute(x, axis, [(i, (i + by) % count) for i in range(count)])


def swapped(x, axis):
    count = lax.axis_size(axis)
    return lax.ppermute(x, axis, [(i, i ^ 1) for i in range(count)])


def body(queries, keys, neg_mask, positive, row_weight):
    logit_scale = 2.0 / math.sqrt(D)
    cycle_size = lax.axis_size("dp")
    cycle_index = lax.axis_index("dp")
    rep_index = lax.axis_index("rep")
    core = cycle_index % 2
    delta = 1 - 2 * core
    query_rows = queries.shape[0]
    tile_rows = keys.shape[0]
    query_blocks = query_rows // tile_rows
    inner_idx = jnp.arange(tile_rows, dtype=jnp.int32)
    same_row = inner_idx[:, None] == inner_idx[None, :]

    down2 = passed_along(keys, "dp", 2)
    up2 = passed_along(keys, "dp", -2)
    down4 = passed_along(down2, "dp", 2)
    up4 = passed_along(up2, "dp", -2)
    sw_own = swapped(keys, "dp")
    sw_down2 = swapped(down2, "dp")
    sw_up2 = swapped(up2, "dp")
    sw_far = swapped(jnp.where(core == 0, up4, down4), "dp")
    key_tiles = [
        ("own", keys, 0),
        ("sw_own", sw_own, delta),
        ("down2", down2, -2),
        ("up2", up2, 2),
        ("sw_down2", sw_down2, delta - 2),
        ("sw_up2", sw_up2, delta + 2),
        ("down4", down4, -4),
        ("up4", up4, 4),
        ("sw_far", sw_far, -3 * delta),
    ]
    run_max = jnp.full((query_rows,), -1e30, jnp.float32)
    run_sum = jnp.zeros((query_rows,), jnp.float32)
    pos_logit = jnp.zeros((query_rows,), jnp.float32)
    stored = []
    for name, key_tile, offset in key_tiles:
        owner_idx = (cycle_index + offset) % cycle_size
        column = lax.dynamic_slice_in_dim(neg_mask, owner_idx, 1, 1)[:, 0]
        hit_block = positive == owner_idx
        allow_block = (column == 1) | hit_block
        allowed = jnp.broadcast_to(
            allow_block[:, None, None], (query_blocks, tile_rows, tile_rows)
        ).reshape(query_rows, tile_rows)
        at_positive = (hit_block[:, None, None] & same_row[None, :, :]).reshape(
            query_rows, tile_rows
        )
        logit_tile = logit_scale * lax.dot_general(
            queries, key_tile, (((1,), (1,)), ((), ())), preferred_element_type=jnp.float32
        )
        masked = jnp.where(allowed, logit_tile, jnp.float32(-1e30))
        next_max = jnp.maximum(run_max, jnp.max(masked, axis=1))
        run_sum = run_sum * jnp.exp(run_max - next_max) + jnp.sum(
            jnp.where(allowed, jnp.exp(masked - next_max[:, None]), 0.0), axis=1
        )
        run_max = next_max
        pos_logit = pos_logit + jnp.sum(jnp.where(at_positive, logit_tile, 0.0), axis=1)
        stored.append((name, key_tile, masked, at_positive))
    log_total = run_max + jnp.log(run_sum)
    row_loss = log_total - pos_logit
    coefficients = []
    for name, key_tile, masked, at_positive in stored:
        softmax_p = jnp.exp(masked - log_total[:, None])
        coefficients.append(
            (row_weight[:, None] * (softmax_p - at_positive.astype(jnp.float32))).astype(jnp.bfloat16)
        )
    coefficient = jnp.concatenate(coefficients, axis=1)
    window = jnp.concatenate([key_tile for _, key_tile, _, _ in stored], axis=0)
    grad_query = logit_scale * jnp.dot(coefficient, window, preferred_element_type=jnp.float32)
    all_parts = lax.dot_general(
        coefficient, queries, (((0,), (0,)), ((), ())), preferred_element_type=jnp.float32
    )
    key_parts = {
        name: all_parts[i * tile_rows : (i + 1) * tile_rows] for i, (name, _, _, _) in enumerate(stored)
    }
    back_own = swapped(key_parts["sw_own"], "dp")
    back_down2 = swapped(key_parts["sw_down2"], "dp")
    back_up2 = swapped(key_parts["sw_up2"], "dp")
    back_far = swapped(key_parts["sw_far"], "dp")
    zero = jnp.zeros_like(back_far)
    far_up = key_parts["up4"] + jnp.where(core == 0, back_far, zero)
    far_down = key_parts["down4"] + jnp.where(core == 0, zero, back_far)
    near_up = key_parts["up2"] + back_up2 + passed_along(far_up, "dp", 2)
    near_down = key_parts["down2"] + back_down2 + passed_along(far_down, "dp", -2)
    total = (
        key_parts["own"]
        + back_own
        + passed_along(near_up, "dp", 2)
        + passed_along(near_down, "dp", -2)
    )
    half = tile_rows // 2
    halves = total.reshape(2, half, total.shape[1])
    mine = jnp.where(rep_index == 0, halves[0], halves[1])
    other = jnp.where(rep_index == 0, halves[1], halves[0])
    grad_keys = logit_scale * (mine + lax.ppermute(other, "rep", [(0, 1), (1, 0)]))
    return (row_loss, grad_query, grad_keys)


def solution(mesh):
    placed = (
        P(("dp", "rep"), None),
        P("dp", None),
        P(("dp", "rep"), None),
        P(("dp", "rep")),
        P(("dp", "rep")),
    )
    return jax.shard_map(
        body,
        mesh=mesh,
        in_specs=placed,
        out_specs=(P(("dp", "rep")), P(("dp", "rep"), None), P(("dp", "rep"), None)),
        check_vma=False,
    )
```

```python
import math

import jax
import jax.numpy as jnp
from jax import lax
from jax.sharding import PartitionSpec as P

D = 1024
REACH = 4


def passed_along(x, axis, by):
    count = lax.axis_size(axis)
    return lax.ppermute(x, axis, [(i, (i + by) % count) for i in range(count)])


def swapped(x, axis):
    count = lax.axis_size(axis)
    return lax.ppermute(x, axis, [(i, i ^ 1) for i in range(count)])


def body(queries, keys, neg_mask, positive, row_weight):
    logit_scale = 2.0 / math.sqrt(D)
    cycle_size = lax.axis_size("dp")
    cycle_index = lax.axis_index("dp")
    rep_index = lax.axis_index("rep")
    core = cycle_index % 2
    delta = 1 - 2 * core
    query_rows = queries.shape[0]
    tile_rows = keys.shape[0]
    query_blocks = query_rows // tile_rows
    inner_idx = jnp.arange(tile_rows, dtype=jnp.int32)
    same_row = inner_idx[:, None] == inner_idx[None, :]

    down2 = passed_along(keys, "dp", 2)
    up2 = passed_along(keys, "dp", -2)
    down4 = passed_along(down2, "dp", 2)
    up4 = passed_along(up2, "dp", -2)
    sw_own = swapped(keys, "dp")
    sw_down2 = swapped(down2, "dp")
    sw_up2 = swapped(up2, "dp")
    sw_far = swapped(jnp.where(core == 0, up4, down4), "dp")
    key_tiles = [
        ("own", keys, 0),
        ("sw_own", sw_own, delta),
        ("down2", down2, -2),
        ("up2", up2, 2),
        ("sw_down2", sw_down2, delta - 2),
        ("sw_up2", sw_up2, delta + 2),
        ("down4", down4, -4),
        ("up4", up4, 4),
        ("sw_far", sw_far, -3 * delta),
    ]
    run_max = jnp.full((query_rows,), -1e30, jnp.float32)
    run_sum = jnp.zeros((query_rows,), jnp.float32)
    pos_logit = jnp.zeros((query_rows,), jnp.float32)
    stored = []
    for name, key_tile, offset in key_tiles:
        owner_idx = (cycle_index + offset) % cycle_size
        column = lax.dynamic_slice_in_dim(neg_mask, owner_idx, 1, 1)[:, 0]
        hit_block = positive == owner_idx
        allow_block = (column == 1) | hit_block
        allowed = jnp.broadcast_to(
            allow_block[:, None, None], (query_blocks, tile_rows, tile_rows)
        ).reshape(query_rows, tile_rows)
        at_positive = (hit_block[:, None, None] & same_row[None, :, :]).reshape(
            query_rows, tile_rows
        )
        logit_tile = logit_scale * lax.dot_general(
            queries, key_tile, (((1,), (1,)), ((), ())), preferred_element_type=jnp.float32
        )
        masked = jnp.where(allowed, logit_tile, jnp.float32(-1e30))
        next_max = jnp.maximum(run_max, jnp.max(masked, axis=1))
        run_sum = run_sum * jnp.exp(run_max - next_max) + jnp.sum(
            jnp.where(allowed, jnp.exp(masked - next_max[:, None]), 0.0), axis=1
        )
        run_max = next_max
        pos_logit = pos_logit + jnp.sum(jnp.where(at_positive, logit_tile, 0.0), axis=1)
        stored.append((name, key_tile, masked, at_positive))
    log_total = run_max + jnp.log(run_sum)
    row_loss = log_total - pos_logit
    coefficients = []
    for name, key_tile, masked, at_positive in stored:
        softmax_p = jnp.exp(masked - log_total[:, None])
        coefficients.append(
            (row_weight[:, None] * (softmax_p - at_positive.astype(jnp.float32))).astype(jnp.bfloat16)
        )
    coefficient = jnp.concatenate(coefficients, axis=1)
    window = jnp.concatenate([key_tile for _, key_tile, _, _ in stored], axis=0)
    grad_query = logit_scale * jnp.dot(coefficient, window, preferred_element_type=jnp.float32)
    all_parts = lax.dot_general(
        coefficient, queries, (((0,), (0,)), ((), ())), preferred_element_type=jnp.float32
    )
    key_parts = {
        name: all_parts[i * tile_rows : (i + 1) * tile_rows] for i, (name, _, _, _) in enumerate(stored)
    }
    back_own = swapped(key_parts["sw_own"], "dp")
    back_down2 = swapped(key_parts["sw_down2"], "dp")
    back_up2 = swapped(key_parts["sw_up2"], "dp")
    back_far = swapped(key_parts["sw_far"], "dp")
    zero = jnp.zeros_like(back_far)
    far_up = key_parts["up4"] + jnp.where(core == 0, back_far, zero)
    far_down = key_parts["down4"] + jnp.where(core == 0, zero, back_far)
    near_up = key_parts["up2"] + back_up2 + passed_along(far_up, "dp", 2)
    near_down = key_parts["down2"] + back_down2 + passed_along(far_down, "dp", -2)
    half = tile_rows // 2
    mine_at = rep_index * half
    other_at = (1 - rep_index) * half

    def rows_at(x, start):
        return lax.dynamic_slice_in_dim(x, start, half, 0)

    own_part = key_parts["own"] + back_own
    rep_count = lax.axis_size("rep")

    def crossed(x, by):
        pairs = []
        for i in range(cycle_size):
            for j in range(rep_count):
                pairs.append((i * rep_count + j, ((i + by) % cycle_size) * rep_count + (1 - j)))
        return lax.ppermute(x, ("dp", "rep"), pairs)

    total = (
        rows_at(own_part, mine_at)
        + lax.ppermute(rows_at(own_part, other_at), "rep", [(0, 1), (1, 0)])
        + passed_along(rows_at(near_up, mine_at), "dp", 2)
        + passed_along(rows_at(near_down, mine_at), "dp", -2)
        + crossed(rows_at(near_up, other_at), 2)
        + crossed(rows_at(near_down, other_at), -2)
    )
    grad_keys = logit_scale * total
    return (row_loss, grad_query, grad_keys)


def solution(mesh):
    placed = (
        P(("dp", "rep"), None),
        P("dp", None),
        P(("dp", "rep"), None),
        P(("dp", "rep")),
        P(("dp", "rep")),
    )
    return jax.shard_map(
        body,
        mesh=mesh,
        in_specs=placed,
        out_specs=(P(("dp", "rep")), P(("dp", "rep"), None), P(("dp", "rep"), None)),
        check_vma=False,
    )
```

```python
import math

import jax
import jax.numpy as jnp
from jax import lax
from jax.sharding import PartitionSpec as P

D = 1024
REACH = 4


def passed_along(x, axis, by):
    count = lax.axis_size(axis)
    return lax.ppermute(x, axis, [(i, (i + by) % count) for i in range(count)])


def swapped(x, axis):
    count = lax.axis_size(axis)
    return lax.ppermute(x, axis, [(i, i ^ 1) for i in range(count)])


def body(queries, keys, neg_mask, positive, row_weight):
    logit_scale = 2.0 / math.sqrt(D)
    cycle_size = lax.axis_size("dp")
    cycle_index = lax.axis_index("dp")
    rep_index = lax.axis_index("rep")
    core = cycle_index % 2
    delta = 1 - 2 * core
    query_rows = queries.shape[0]
    tile_rows = keys.shape[0]
    query_blocks = query_rows // tile_rows
    inner_idx = jnp.arange(tile_rows, dtype=jnp.int32)
    same_row = inner_idx[:, None] == inner_idx[None, :]

    down2 = passed_along(keys, "dp", 2)
    up2 = passed_along(keys, "dp", -2)
    down4 = passed_along(down2, "dp", 2)
    up4 = passed_along(up2, "dp", -2)
    sw_own = swapped(keys, "dp")
    sw_down2 = swapped(down2, "dp")
    sw_up2 = swapped(up2, "dp")
    sw_far = swapped(jnp.where(core == 0, up4, down4), "dp")
    key_tiles = [
        ("own", keys, 0),
        ("sw_own", sw_own, delta),
        ("down2", down2, -2),
        ("up2", up2, 2),
        ("sw_down2", sw_down2, delta - 2),
        ("sw_up2", sw_up2, delta + 2),
        ("down4", down4, -4),
        ("up4", up4, 4),
        ("sw_far", sw_far, -3 * delta),
    ]
    run_max = jnp.full((query_rows,), -1e30, jnp.float32)
    run_sum = jnp.zeros((query_rows,), jnp.float32)
    pos_logit = jnp.zeros((query_rows,), jnp.float32)
    stored = []
    for name, key_tile, offset in key_tiles:
        owner_idx = (cycle_index + offset) % cycle_size
        column = lax.dynamic_slice_in_dim(neg_mask, owner_idx, 1, 1)[:, 0]
        hit_block = positive == owner_idx
        allow_block = (column == 1) | hit_block
        allowed = jnp.broadcast_to(
            allow_block[:, None, None], (query_blocks, tile_rows, tile_rows)
        ).reshape(query_rows, tile_rows)
        at_positive = (hit_block[:, None, None] & same_row[None, :, :]).reshape(
            query_rows, tile_rows
        )
        logit_tile = logit_scale * lax.dot_general(
            queries, key_tile, (((1,), (1,)), ((), ())), preferred_element_type=jnp.float32
        )
        masked = jnp.where(allowed, logit_tile, jnp.float32(-1e30))
        next_max = jnp.maximum(run_max, jnp.max(masked, axis=1))
        run_sum = run_sum * jnp.exp(run_max - next_max) + jnp.sum(
            jnp.where(allowed, jnp.exp(masked - next_max[:, None]), 0.0), axis=1
        )
        run_max = next_max
        pos_logit = pos_logit + jnp.sum(jnp.where(at_positive, logit_tile, 0.0), axis=1)
        stored.append((name, key_tile, masked, at_positive))
    log_total = run_max + jnp.log(run_sum)
    row_loss = log_total - pos_logit
    coefficients = []
    for name, key_tile, masked, at_positive in stored:
        softmax_p = jnp.exp(masked - log_total[:, None])
        coefficients.append(
            (row_weight[:, None] * (softmax_p - at_positive.astype(jnp.float32))).astype(jnp.bfloat16)
        )
    coefficient = jnp.concatenate(coefficients, axis=1)
    window = jnp.concatenate([key_tile for _, key_tile, _, _ in stored], axis=0)
    grad_query = logit_scale * jnp.dot(coefficient, window, preferred_element_type=jnp.float32)
    all_parts = lax.dot_general(
        coefficient, queries, (((0,), (0,)), ((), ())), preferred_element_type=jnp.float32
    )
    key_parts = {
        name: all_parts[i * tile_rows : (i + 1) * tile_rows] for i, (name, _, _, _) in enumerate(stored)
    }
    back_own = swapped(key_parts["sw_own"], "dp")
    back_down2 = swapped(key_parts["sw_down2"], "dp")
    back_up2 = swapped(key_parts["sw_up2"], "dp")
    back_far = swapped(key_parts["sw_far"], "dp")
    zero = jnp.zeros_like(back_far)
    far_up = key_parts["up4"] + jnp.where(core == 0, back_far, zero)
    far_down = key_parts["down4"] + jnp.where(core == 0, zero, back_far)
    near_up = key_parts["up2"] + back_up2 + passed_along(far_up, "dp", 2)
    near_down = key_parts["down2"] + back_down2 + passed_along(far_down, "dp", -2)
    near_up, near_down, grad_query = lax.optimization_barrier((near_up, near_down, grad_query))
    total = (
        key_parts["own"]
        + back_own
        + passed_along(near_up, "dp", 2)
        + passed_along(near_down, "dp", -2)
    )
    half = tile_rows // 2
    halves = total.reshape(2, half, total.shape[1])
    mine = jnp.where(rep_index == 0, halves[0], halves[1])
    other = jnp.where(rep_index == 0, halves[1], halves[0])
    grad_keys = logit_scale * (mine + lax.ppermute(other, "rep", [(0, 1), (1, 0)]))
    return (row_loss, grad_query, grad_keys)


def solution(mesh):
    placed = (
        P(("dp", "rep"), None),
        P("dp", None),
        P(("dp", "rep"), None),
        P(("dp", "rep")),
        P(("dp", "rep")),
    )
    return jax.shard_map(
        body,
        mesh=mesh,
        in_specs=placed,
        out_specs=(P(("dp", "rep")), P(("dp", "rep"), None), P(("dp", "rep"), None)),
        check_vma=False,
    )
```

```python
import math

import jax
import jax.numpy as jnp
from jax import lax
from jax.sharding import PartitionSpec as P

D = 1024
REACH = 4


def passed_along(x, axis, by):
    count = lax.axis_size(axis)
    return lax.ppermute(x, axis, [(i, (i + by) % count) for i in range(count)])


def swapped(x, axis):
    count = lax.axis_size(axis)
    return lax.ppermute(x, axis, [(i, i ^ 1) for i in range(count)])


def body(queries, keys, neg_mask, positive, row_weight):
    logit_scale = 2.0 / math.sqrt(D)
    cycle_size = lax.axis_size("dp")
    cycle_index = lax.axis_index("dp")
    rep_index = lax.axis_index("rep")
    core = cycle_index % 2
    delta = 1 - 2 * core
    query_rows = queries.shape[0]
    tile_rows = keys.shape[0]
    query_blocks = query_rows // tile_rows
    inner_idx = jnp.arange(tile_rows, dtype=jnp.int32)
    same_row = inner_idx[:, None] == inner_idx[None, :]

    def ring(x, forward):
        pairs = []
        for i in range(cycle_size):
            step = 2 if (i % 2 == 0) == forward else -2
            pairs.append((i, (i + step) % cycle_size))
        return lax.ppermute(x, "dp", pairs)

    partner_keys = swapped(keys, "dp")
    pair = jnp.where(
        core == 0,
        jnp.concatenate([keys, partner_keys], axis=0),
        jnp.concatenate([partner_keys, keys], axis=0),
    )
    recv1 = ring(pair, True)
    recv2 = ring(recv1, True)
    side1 = swapped(recv1, "dp")
    side2 = swapped(jnp.where(core == 0, recv2[tile_rows:], recv2[:tile_rows]), "dp")
    key_tiles = [
        ("pair0", pair[:tile_rows], -core),
        ("pair1", pair[tile_rows:], 1 - core),
        ("r1_0", recv1[:tile_rows], -2 * delta - core),
        ("r1_1", recv1[tile_rows:], -2 * delta + 1 - core),
        ("r2_0", recv2[:tile_rows], -4 * delta - core),
        ("r2_1", recv2[tile_rows:], -4 * delta + 1 - core),
        ("s1_0", side1[:tile_rows], 2 * delta - core),
        ("s1_1", side1[tile_rows:], 2 * delta + 1 - core),
        ("s2", side2, 4 * delta),
    ]
    run_max = jnp.full((query_rows,), -1e30, jnp.float32)
    run_sum = jnp.zeros((query_rows,), jnp.float32)
    pos_logit = jnp.zeros((query_rows,), jnp.float32)
    stored = []
    for name, key_tile, offset in key_tiles:
        owner_idx = (cycle_index + offset) % cycle_size
        column = lax.dynamic_slice_in_dim(neg_mask, owner_idx, 1, 1)[:, 0]
        hit_block = positive == owner_idx
        allow_block = (column == 1) | hit_block
        allowed = jnp.broadcast_to(
            allow_block[:, None, None], (query_blocks, tile_rows, tile_rows)
        ).reshape(query_rows, tile_rows)
        at_positive = (hit_block[:, None, None] & same_row[None, :, :]).reshape(
            query_rows, tile_rows
        )
        logit_tile = logit_scale * lax.dot_general(
            queries, key_tile, (((1,), (1,)), ((), ())), preferred_element_type=jnp.float32
        )
        masked = jnp.where(allowed, logit_tile, jnp.float32(-1e30))
        next_max = jnp.maximum(run_max, jnp.max(masked, axis=1))
        run_sum = run_sum * jnp.exp(run_max - next_max) + jnp.sum(
            jnp.where(allowed, jnp.exp(masked - next_max[:, None]), 0.0), axis=1
        )
        run_max = next_max
        pos_logit = pos_logit + jnp.sum(jnp.where(at_positive, logit_tile, 0.0), axis=1)
        stored.append((name, key_tile, masked, at_positive))
    log_total = run_max + jnp.log(run_sum)
    row_loss = log_total - pos_logit
    coefficients = []
    for name, key_tile, masked, at_positive in stored:
        softmax_p = jnp.exp(masked - log_total[:, None])
        coefficients.append(
            (row_weight[:, None] * (softmax_p - at_positive.astype(jnp.float32))).astype(jnp.bfloat16)
        )
    coefficient = jnp.concatenate(coefficients, axis=1)
    window = jnp.concatenate([key_tile for _, key_tile, _, _ in stored], axis=0)
    grad_query = logit_scale * jnp.dot(coefficient, window, preferred_element_type=jnp.float32)
    all_parts = lax.dot_general(
        coefficient, queries, (((0,), (0,)), ((), ())), preferred_element_type=jnp.float32
    )
    t = tile_rows
    part_pair = all_parts[0 : 2 * t]
    part_r1 = all_parts[2 * t : 4 * t]
    part_r2 = all_parts[4 * t : 6 * t]
    part_s1 = all_parts[6 * t : 8 * t]
    part_s2 = all_parts[8 * t : 9 * t]
    back_s2 = swapped(part_s2, "dp")
    zero = jnp.zeros_like(back_s2)
    full_r2 = part_r2 + jnp.where(
        core == 1,
        jnp.concatenate([back_s2, zero], axis=0),
        jnp.concatenate([zero, back_s2], axis=0),
    )
    full_r1 = part_r1 + swapped(part_s1, "dp") + ring(full_r2, False)
    full_pair = part_pair + ring(full_r1, False)
    mine = jnp.where(core == 0, full_pair[:t], full_pair[t:])
    other = jnp.where(core == 0, full_pair[t:], full_pair[:t])
    total = mine + swapped(other, "dp")
    half = t // 2
    halves = total.reshape(2, half, total.shape[1])
    mine_half = jnp.where(rep_index == 0, halves[0], halves[1])
    other_half = jnp.where(rep_index == 0, halves[1], halves[0])
    grad_keys = logit_scale * (mine_half + lax.ppermute(other_half, "rep", [(0, 1), (1, 0)]))
    return (row_loss, grad_query, grad_keys)


def solution(mesh):
    placed = (
        P(("dp", "rep"), None),
        P("dp", None),
        P(("dp", "rep"), None),
        P(("dp", "rep")),
        P(("dp", "rep")),
    )
    return jax.shard_map(
        body,
        mesh=mesh,
        in_specs=placed,
        out_specs=(P(("dp", "rep")), P(("dp", "rep"), None), P(("dp", "rep"), None)),
        check_vma=False,
    )
```

```python
import math

import jax
import jax.numpy as jnp
from jax import lax
from jax.sharding import PartitionSpec as P

D = 1024
REACH = 4


def passed_along(x, axis, by):
    count = lax.axis_size(axis)
    return lax.ppermute(x, axis, [(i, (i + by) % count) for i in range(count)])


def swapped(x, axis):
    count = lax.axis_size(axis)
    return lax.ppermute(x, axis, [(i, i ^ 1) for i in range(count)])


def body(queries, keys, neg_mask, positive, row_weight):
    logit_scale = 2.0 / math.sqrt(D)
    cycle_size = lax.axis_size("dp")
    cycle_index = lax.axis_index("dp")
    rep_index = lax.axis_index("rep")
    core = cycle_index % 2
    delta = 1 - 2 * core
    query_rows = queries.shape[0]
    tile_rows = keys.shape[0]
    query_blocks = query_rows // tile_rows
    inner_idx = jnp.arange(tile_rows, dtype=jnp.int32)
    same_row = inner_idx[:, None] == inner_idx[None, :]

    down2 = passed_along(keys, "dp", 2)
    up2 = passed_along(keys, "dp", -2)
    down4 = passed_along(down2, "dp", 2)
    up4 = passed_along(up2, "dp", -2)
    sw_own = swapped(keys, "dp")
    sw_near = swapped(jnp.concatenate([down2, up2], axis=0), "dp")
    sw_down2 = sw_near[:tile_rows]
    sw_up2 = sw_near[tile_rows:]
    sw_far = swapped(jnp.where(core == 0, up4, down4), "dp")
    key_tiles = [
        ("own", keys, 0),
        ("sw_own", sw_own, delta),
        ("down2", down2, -2),
        ("up2", up2, 2),
        ("sw_down2", sw_down2, delta - 2),
        ("sw_up2", sw_up2, delta + 2),
        ("down4", down4, -4),
        ("up4", up4, 4),
        ("sw_far", sw_far, -3 * delta),
    ]
    run_max = jnp.full((query_rows,), -1e30, jnp.float32)
    run_sum = jnp.zeros((query_rows,), jnp.float32)
    pos_logit = jnp.zeros((query_rows,), jnp.float32)
    stored = []
    for name, key_tile, offset in key_tiles:
        owner_idx = (cycle_index + offset) % cycle_size
        column = lax.dynamic_slice_in_dim(neg_mask, owner_idx, 1, 1)[:, 0]
        hit_block = positive == owner_idx
        allow_block = (column == 1) | hit_block
        allowed = jnp.broadcast_to(
            allow_block[:, None, None], (query_blocks, tile_rows, tile_rows)
        ).reshape(query_rows, tile_rows)
        at_positive = (hit_block[:, None, None] & same_row[None, :, :]).reshape(
            query_rows, tile_rows
        )
        logit_tile = logit_scale * lax.dot_general(
            queries, key_tile, (((1,), (1,)), ((), ())), preferred_element_type=jnp.float32
        )
        masked = jnp.where(allowed, logit_tile, jnp.float32(-1e30))
        next_max = jnp.maximum(run_max, jnp.max(masked, axis=1))
        run_sum = run_sum * jnp.exp(run_max - next_max) + jnp.sum(
            jnp.where(allowed, jnp.exp(masked - next_max[:, None]), 0.0), axis=1
        )
        run_max = next_max
        pos_logit = pos_logit + jnp.sum(jnp.where(at_positive, logit_tile, 0.0), axis=1)
        stored.append((name, key_tile, masked, at_positive))
    log_total = run_max + jnp.log(run_sum)
    row_loss = log_total - pos_logit
    coefficients = []
    for name, key_tile, masked, at_positive in stored:
        softmax_p = jnp.exp(masked - log_total[:, None])
        coefficients.append(
            (row_weight[:, None] * (softmax_p - at_positive.astype(jnp.float32))).astype(jnp.bfloat16)
        )
    coefficient = jnp.concatenate(coefficients, axis=1)
    window = jnp.concatenate([key_tile for _, key_tile, _, _ in stored], axis=0)
    grad_query = logit_scale * jnp.dot(coefficient, window, preferred_element_type=jnp.float32)
    first = ("sw_own", "sw_down2", "sw_up2", "down4", "up4", "sw_far")
    order = {name: i for i, (name, _, _, _) in enumerate(stored)}

    def parts_of(names):
        cols = jnp.concatenate([coefficients[order[n]] for n in names], axis=1)
        out = lax.dot_general(
            cols, queries, (((0,), (0,)), ((), ())), preferred_element_type=jnp.float32
        )
        return {n: out[i * tile_rows : (i + 1) * tile_rows] for i, n in enumerate(names)}

    key_parts = parts_of(first)
    key_parts.update(parts_of(("own", "down2", "up2")))
    backs = swapped(
        jnp.concatenate([key_parts[n] for n in ("sw_own", "sw_down2", "sw_up2", "sw_far")], axis=0),
        "dp",
    )
    back_own = backs[:tile_rows]
    back_down2 = backs[tile_rows : 2 * tile_rows]
    back_up2 = backs[2 * tile_rows : 3 * tile_rows]
    back_far = backs[3 * tile_rows :]
    zero = jnp.zeros_like(back_far)
    far_up = key_parts["up4"] + jnp.where(core == 0, back_far, zero)
    far_down = key_parts["down4"] + jnp.where(core == 0, zero, back_far)
    near_up = key_parts["up2"] + back_up2 + passed_along(far_up, "dp", 2)
    near_down = key_parts["down2"] + back_down2 + passed_along(far_down, "dp", -2)
    total = (
        key_parts["own"]
        + back_own
        + passed_along(near_up, "dp", 2)
        + passed_along(near_down, "dp", -2)
    )
    half = tile_rows // 2
    halves = total.reshape(2, half, total.shape[1])
    mine = jnp.where(rep_index == 0, halves[0], halves[1])
    other = jnp.where(rep_index == 0, halves[1], halves[0])
    grad_keys = logit_scale * (mine + lax.ppermute(other, "rep", [(0, 1), (1, 0)]))
    return (row_loss, grad_query, grad_keys)


def solution(mesh):
    placed = (
        P(("dp", "rep"), None),
        P("dp", None),
        P(("dp", "rep"), None),
        P(("dp", "rep")),
        P(("dp", "rep")),
    )
    return jax.shard_map(
        body,
        mesh=mesh,
        in_specs=placed,
        out_specs=(P(("dp", "rep")), P(("dp", "rep"), None), P(("dp", "rep"), None)),
        check_vma=False,
    )
```

```python
import math

import jax
import jax.numpy as jnp
from jax import lax
from jax.sharding import PartitionSpec as P

D = 1024
REACH = 4


def passed_along(x, axis, by):
    count = lax.axis_size(axis)
    return lax.ppermute(x, axis, [(i, (i + by) % count) for i in range(count)])


def swapped(x, axis):
    count = lax.axis_size(axis)
    return lax.ppermute(x, axis, [(i, i ^ 1) for i in range(count)])


def body(queries, keys, neg_mask, positive, row_weight):
    logit_scale = 2.0 / math.sqrt(D)
    cycle_size = lax.axis_size("dp")
    cycle_index = lax.axis_index("dp")
    rep_index = lax.axis_index("rep")
    core = cycle_index % 2
    delta = 1 - 2 * core
    query_rows = queries.shape[0]
    tile_rows = keys.shape[0]
    query_blocks = query_rows // tile_rows
    inner_idx = jnp.arange(tile_rows, dtype=jnp.int32)
    same_row = inner_idx[:, None] == inner_idx[None, :]

    up2 = passed_along(keys, "dp", -2)
    down2 = passed_along(keys, "dp", 2)
    up4 = passed_along(up2, "dp", -2)
    down4 = passed_along(down2, "dp", 2)
    sw_own = swapped(keys, "dp")
    sw_down2 = swapped(down2, "dp")
    sw_up2 = swapped(up2, "dp")
    sw_far = swapped(jnp.where(core == 0, up4, down4), "dp")
    key_tiles = [
        ("own", keys, 0),
        ("sw_own", sw_own, delta),
        ("down2", down2, -2),
        ("up2", up2, 2),
        ("sw_down2", sw_down2, delta - 2),
        ("sw_up2", sw_up2, delta + 2),
        ("down4", down4, -4),
        ("up4", up4, 4),
        ("sw_far", sw_far, -3 * delta),
    ]
    run_max = jnp.full((query_rows,), -1e30, jnp.float32)
    run_sum = jnp.zeros((query_rows,), jnp.float32)
    pos_logit = jnp.zeros((query_rows,), jnp.float32)
    stored = []
    for name, key_tile, offset in key_tiles:
        owner_idx = (cycle_index + offset) % cycle_size
        column = lax.dynamic_slice_in_dim(neg_mask, owner_idx, 1, 1)[:, 0]
        hit_block = positive == owner_idx
        allow_block = (column == 1) | hit_block
        allowed = jnp.broadcast_to(
            allow_block[:, None, None], (query_blocks, tile_rows, tile_rows)
        ).reshape(query_rows, tile_rows)
        at_positive = (hit_block[:, None, None] & same_row[None, :, :]).reshape(
            query_rows, tile_rows
        )
        logit_tile = logit_scale * lax.dot_general(
            queries, key_tile, (((1,), (1,)), ((), ())), preferred_element_type=jnp.float32
        )
        masked = jnp.where(allowed, logit_tile, jnp.float32(-1e30))
        next_max = jnp.maximum(run_max, jnp.max(masked, axis=1))
        run_sum = run_sum * jnp.exp(run_max - next_max) + jnp.sum(
            jnp.where(allowed, jnp.exp(masked - next_max[:, None]), 0.0), axis=1
        )
        run_max = next_max
        pos_logit = pos_logit + jnp.sum(jnp.where(at_positive, logit_tile, 0.0), axis=1)
        stored.append((name, key_tile, masked, at_positive))
    log_total = run_max + jnp.log(run_sum)
    row_loss = log_total - pos_logit
    coefficients = []
    for name, key_tile, masked, at_positive in stored:
        softmax_p = jnp.exp(masked - log_total[:, None])
        coefficients.append(
            (row_weight[:, None] * (softmax_p - at_positive.astype(jnp.float32))).astype(jnp.bfloat16)
        )
    coefficient = jnp.concatenate(coefficients, axis=1)
    window = jnp.concatenate([key_tile for _, key_tile, _, _ in stored], axis=0)
    grad_query = logit_scale * jnp.dot(coefficient, window, preferred_element_type=jnp.float32)
    all_parts = lax.dot_general(
        coefficient, queries, (((0,), (0,)), ((), ())), preferred_element_type=jnp.float32
    )
    key_parts = {
        name: all_parts[i * tile_rows : (i + 1) * tile_rows] for i, (name, _, _, _) in enumerate(stored)
    }
    back_own = swapped(key_parts["sw_own"], "dp")
    back_down2 = swapped(key_parts["sw_down2"], "dp")
    back_up2 = swapped(key_parts["sw_up2"], "dp")
    back_far = swapped(key_parts["sw_far"], "dp")
    zero = jnp.zeros_like(back_far)
    far_up = key_parts["up4"] + jnp.where(core == 0, back_far, zero)
    far_down = key_parts["down4"] + jnp.where(core == 0, zero, back_far)
    near_down = key_parts["down2"] + back_down2 + passed_along(far_down, "dp", -2)
    near_up = key_parts["up2"] + back_up2 + passed_along(far_up, "dp", 2)
    total = (
        key_parts["own"]
        + back_own
        + passed_along(near_down, "dp", -2)
        + passed_along(near_up, "dp", 2)
    )
    half = tile_rows // 2
    halves = total.reshape(2, half, total.shape[1])
    mine = jnp.where(rep_index == 0, halves[0], halves[1])
    other = jnp.where(rep_index == 0, halves[1], halves[0])
    grad_keys = logit_scale * (mine + lax.ppermute(other, "rep", [(0, 1), (1, 0)]))
    return (row_loss, grad_query, grad_keys)


def solution(mesh):
    placed = (
        P(("dp", "rep"), None),
        P("dp", None),
        P(("dp", "rep"), None),
        P(("dp", "rep")),
        P(("dp", "rep")),
    )
    return jax.shard_map(
        body,
        mesh=mesh,
        in_specs=placed,
        out_specs=(P(("dp", "rep")), P(("dp", "rep"), None), P(("dp", "rep"), None)),
        check_vma=False,
    )
```

```python
import math

import jax
import jax.numpy as jnp
from jax import lax
from jax.sharding import PartitionSpec as P


D = 1024


def passed_along(x, axis, by):
    count = lax.axis_size(axis)
    return lax.ppermute(x, axis, [(i, (i + by) % count) for i in range(count)])


def swapped(x, axis):
    count = lax.axis_size(axis)
    return lax.ppermute(x, axis, [(i, i ^ 1) for i in range(count)])


def step(queries, keys, neg_mask, positive, row_weight):
    logit_scale = 2.0 / math.sqrt(D)
    cycle_size = lax.axis_size("dp")
    cycle_index = lax.axis_index("dp")
    rep_index = lax.axis_index("rep")
    core = cycle_index % 2
    delta = 1 - 2 * core
    query_rows = queries.shape[0]
    tile_rows = keys.shape[0]
    query_blocks = query_rows // tile_rows
    inner_idx = jnp.arange(tile_rows, dtype=jnp.int32)
    same_row = inner_idx[:, None] == inner_idx[None, :]

    down2 = passed_along(keys, "dp", 2)
    up2 = passed_along(keys, "dp", -2)
    down4 = passed_along(down2, "dp", 2)
    up4 = passed_along(up2, "dp", -2)
    sw_own = swapped(keys, "dp")
    sw_down2 = swapped(down2, "dp")
    sw_up2 = swapped(up2, "dp")
    sw_far = swapped(jnp.where(core == 0, up4, down4), "dp")
    key_tiles = [
        ("own", keys, 0),
        ("sw_own", sw_own, delta),
        ("down2", down2, -2),
        ("up2", up2, 2),
        ("sw_down2", sw_down2, delta - 2),
        ("sw_up2", sw_up2, delta + 2),
        ("down4", down4, -4),
        ("up4", up4, 4),
        ("sw_far", sw_far, -3 * delta),
    ]
    run_max = jnp.full((query_rows,), -1e30, jnp.float32)
    run_sum = jnp.zeros((query_rows,), jnp.float32)
    pos_logit = jnp.zeros((query_rows,), jnp.float32)
    stored = []
    for name, key_tile, offset in key_tiles:
        owner_idx = (cycle_index + offset) % cycle_size
        column = lax.dynamic_slice_in_dim(neg_mask, owner_idx, 1, 1)[:, 0]
        hit_block = positive == owner_idx
        allow_block = (column == 1) | hit_block
        allowed = jnp.broadcast_to(
            allow_block[:, None, None], (query_blocks, tile_rows, tile_rows)
        ).reshape(query_rows, tile_rows)
        at_positive = (hit_block[:, None, None] & same_row[None, :, :]).reshape(
            query_rows, tile_rows
        )
        logit_tile = logit_scale * lax.dot_general(
            queries, key_tile, (((1,), (1,)), ((), ())), preferred_element_type=jnp.float32
        )
        masked = jnp.where(allowed, logit_tile, jnp.float32(-1e30))
        next_max = jnp.maximum(run_max, jnp.max(masked, axis=1))
        run_sum = run_sum * jnp.exp(run_max - next_max) + jnp.sum(
            jnp.where(allowed, jnp.exp(masked - next_max[:, None]), 0.0), axis=1
        )
        run_max = next_max
        pos_logit = pos_logit + jnp.sum(jnp.where(at_positive, logit_tile, 0.0), axis=1)
        stored.append((name, key_tile, masked, at_positive))
    log_total = run_max + jnp.log(run_sum)
    row_loss = log_total - pos_logit
    coefficients = []
    for name, key_tile, masked, at_positive in stored:
        softmax_p = jnp.exp(masked - log_total[:, None])
        coefficients.append(
            (row_weight[:, None] * (softmax_p - at_positive.astype(jnp.float32))).astype(jnp.bfloat16)
        )
    coefficient = jnp.concatenate(coefficients, axis=1)
    window = jnp.concatenate([key_tile for _, key_tile, _, _ in stored], axis=0)
    grad_query = logit_scale * jnp.dot(coefficient, window, preferred_element_type=jnp.float32)
    order = {name: i for i, (name, _, _, _) in enumerate(stored)}

    def parts_of(names):
        cols = jnp.concatenate([coefficients[order[n]] for n in names], axis=1)
        out = lax.dot_general(
            cols, queries, (((0,), (0,)), ((), ())), preferred_element_type=jnp.float32
        )
        return {n: out[i * tile_rows : (i + 1) * tile_rows] for i, n in enumerate(names)}

    key_parts = parts_of(("sw_far", "up4", "down4"))
    key_parts.update(parts_of(("own", "sw_own", "down2", "up2", "sw_down2", "sw_up2")))
    back_own = swapped(key_parts["sw_own"], "dp")
    back_down2 = swapped(key_parts["sw_down2"], "dp")
    back_up2 = swapped(key_parts["sw_up2"], "dp")
    back_far = swapped(key_parts["sw_far"], "dp")
    zero = jnp.zeros_like(back_far)
    far_up = key_parts["up4"] + jnp.where(core == 0, back_far, zero)
    far_down = key_parts["down4"] + jnp.where(core == 0, zero, back_far)
    far_up_in = passed_along(far_up, "dp", 2)
    far_down_in = passed_along(far_down, "dp", -2)
    near_up = key_parts["up2"] + back_up2 + far_up_in
    near_down = key_parts["down2"] + back_down2 + far_down_in
    total = (
        key_parts["own"]
        + back_own
        + passed_along(near_up, "dp", 2)
        + passed_along(near_down, "dp", -2)
    )
    half = tile_rows // 2
    halves = total.reshape(2, half, total.shape[1])
    mine = jnp.where(rep_index == 0, halves[0], halves[1])
    other = jnp.where(rep_index == 0, halves[1], halves[0])
    grad_keys = logit_scale * (mine + lax.ppermute(other, "rep", [(0, 1), (1, 0)]))
    return (row_loss, grad_query, grad_keys)


def solution(mesh):
    placed = (
        P(("dp", "rep"), None),
        P("dp", None),
        P(("dp", "rep"), None),
        P(("dp", "rep")),
        P(("dp", "rep")),
    )
    return jax.shard_map(
        step,
        mesh=mesh,
        in_specs=placed,
        out_specs=(P(("dp", "rep")), P(("dp", "rep"), None), P(("dp", "rep"), None)),
        check_vma=False,
    )
```

```python
import math

import jax
import jax.numpy as jnp
from jax import lax
from jax.sharding import PartitionSpec as P


D = 1024


def passed_along(x, axis, by):
    count = lax.axis_size(axis)
    return lax.ppermute(x, axis, [(i, (i + by) % count) for i in range(count)])


def swapped(x, axis):
    count = lax.axis_size(axis)
    return lax.ppermute(x, axis, [(i, i ^ 1) for i in range(count)])


def step(queries, keys, neg_mask, positive, row_weight):
    logit_scale = 2.0 / math.sqrt(D)
    cycle_size = lax.axis_size("dp")
    cycle_index = lax.axis_index("dp")
    rep_index = lax.axis_index("rep")
    core = cycle_index % 2
    delta = 1 - 2 * core
    query_rows = queries.shape[0]
    tile_rows = keys.shape[0]
    query_blocks = query_rows // tile_rows
    inner_idx = jnp.arange(tile_rows, dtype=jnp.int32)
    same_row = inner_idx[:, None] == inner_idx[None, :]

    down2 = passed_along(keys, "dp", 2)
    up2 = passed_along(keys, "dp", -2)
    down4 = passed_along(down2, "dp", 2)
    up4 = passed_along(up2, "dp", -2)
    sw_own = swapped(keys, "dp")
    sw_down2 = swapped(down2, "dp")
    sw_up2 = swapped(up2, "dp")
    sw_far = swapped(jnp.where(core == 0, up4, down4), "dp")
    key_tiles = [
        ("own", keys, 0),
        ("sw_own", sw_own, delta),
        ("down2", down2, -2),
        ("up2", up2, 2),
        ("sw_down2", sw_down2, delta - 2),
        ("sw_up2", sw_up2, delta + 2),
        ("down4", down4, -4),
        ("up4", up4, 4),
        ("sw_far", sw_far, -3 * delta),
    ]
    run_max = jnp.full((query_rows,), -1e30, jnp.float32)
    run_sum = jnp.zeros((query_rows,), jnp.float32)
    pos_logit = jnp.zeros((query_rows,), jnp.float32)
    stored = []
    for name, key_tile, offset in key_tiles:
        owner_idx = (cycle_index + offset) % cycle_size
        column = lax.dynamic_slice_in_dim(neg_mask, owner_idx, 1, 1)[:, 0]
        hit_block = positive == owner_idx
        allow_block = (column == 1) | hit_block
        allowed = jnp.broadcast_to(
            allow_block[:, None, None], (query_blocks, tile_rows, tile_rows)
        ).reshape(query_rows, tile_rows)
        at_positive = (hit_block[:, None, None] & same_row[None, :, :]).reshape(
            query_rows, tile_rows
        )
        logit_tile = logit_scale * lax.dot_general(
            queries, key_tile, (((1,), (1,)), ((), ())), preferred_element_type=jnp.float32
        )
        masked = jnp.where(allowed, logit_tile, jnp.float32(-1e30))
        next_max = jnp.maximum(run_max, jnp.max(masked, axis=1))
        run_sum = run_sum * jnp.exp(run_max - next_max) + jnp.sum(
            jnp.where(allowed, jnp.exp(masked - next_max[:, None]), 0.0), axis=1
        )
        run_max = next_max
        pos_logit = pos_logit + jnp.sum(jnp.where(at_positive, logit_tile, 0.0), axis=1)
        stored.append((name, key_tile, masked, at_positive))
    log_total = run_max + jnp.log(run_sum)
    row_loss = log_total - pos_logit
    coefficients = []
    for name, key_tile, masked, at_positive in stored:
        softmax_p = jnp.exp(masked - log_total[:, None])
        coefficients.append(
            (row_weight[:, None] * (softmax_p - at_positive.astype(jnp.float32))).astype(jnp.bfloat16)
        )
    coefficient = jnp.concatenate(coefficients, axis=1)
    window = jnp.concatenate([key_tile for _, key_tile, _, _ in stored], axis=0)
    grad_query = logit_scale * jnp.dot(coefficient, window, preferred_element_type=jnp.float32)
    order = {name: i for i, (name, _, _, _) in enumerate(stored)}

    def parts_of(names):
        cols = jnp.concatenate([coefficients[order[n]] for n in names], axis=1)
        out = lax.dot_general(
            cols, queries, (((0,), (0,)), ((), ())), preferred_element_type=jnp.float32
        )
        return {n: out[i * tile_rows : (i + 1) * tile_rows] for i, n in enumerate(names)}

    key_parts = parts_of(("sw_far", "up4", "down4"))
    key_parts.update(parts_of(("own", "sw_own", "down2", "up2", "sw_down2", "sw_up2")))
    back_own = swapped(key_parts["sw_own"], "dp")
    back_down2 = swapped(key_parts["sw_down2"], "dp")
    back_up2 = swapped(key_parts["sw_up2"], "dp")
    back_far = swapped(key_parts["sw_far"], "dp")
    zero = jnp.zeros_like(back_far)
    far_up = key_parts["up4"] + jnp.where(core == 0, back_far, zero)
    far_down = key_parts["down4"] + jnp.where(core == 0, zero, back_far)
    far_up_in = passed_along(far_up, "dp", 2)
    far_down_in = passed_along(far_down, "dp", -2)
    near_up = key_parts["up2"] + back_up2 + far_up_in
    near_down = key_parts["down2"] + back_down2 + far_down_in
    parts = (
        key_parts["own"],
        back_own,
        passed_along(near_up, "dp", 2),
        passed_along(near_down, "dp", -2),
    )
    half = tile_rows // 2
    mine_at = rep_index * half
    other_at = (1 - rep_index) * half
    other = sum(lax.dynamic_slice_in_dim(p, other_at, half, 0) for p in parts[1:]) + lax.dynamic_slice_in_dim(
        parts[0], other_at, half, 0
    )
    received = lax.ppermute(other, "rep", [(0, 1), (1, 0)])
    mine = sum(lax.dynamic_slice_in_dim(p, mine_at, half, 0) for p in parts[1:]) + lax.dynamic_slice_in_dim(
        parts[0], mine_at, half, 0
    )
    grad_keys = logit_scale * (mine + received)
    return (row_loss, grad_query, grad_keys)


def solution(mesh):
    placed = (
        P(("dp", "rep"), None),
        P("dp", None),
        P(("dp", "rep"), None),
        P(("dp", "rep")),
        P(("dp", "rep")),
    )
    return jax.shard_map(
        step,
        mesh=mesh,
        in_specs=placed,
        out_specs=(P(("dp", "rep")), P(("dp", "rep"), None), P(("dp", "rep"), None)),
        check_vma=False,
    )
```

```python
import math

import jax
import jax.numpy as jnp
from jax import lax
from jax.sharding import PartitionSpec as P


D = 1024


def passed_along(x, axis, by):
    count = lax.axis_size(axis)
    return lax.ppermute(x, axis, [(i, (i + by) % count) for i in range(count)])


def swapped(x, axis):
    count = lax.axis_size(axis)
    return lax.ppermute(x, axis, [(i, i ^ 1) for i in range(count)])


def step(queries, keys, neg_mask, positive, row_weight):
    logit_scale = 2.0 / math.sqrt(D)
    cycle_size = lax.axis_size("dp")
    cycle_index = lax.axis_index("dp")
    rep_index = lax.axis_index("rep")
    core = cycle_index % 2
    delta = 1 - 2 * core
    query_rows = queries.shape[0]
    tile_rows = keys.shape[0]
    query_blocks = query_rows // tile_rows
    inner_idx = jnp.arange(tile_rows, dtype=jnp.int32)
    same_row = inner_idx[:, None] == inner_idx[None, :]

    down2 = passed_along(keys, "dp", 2)
    up2 = passed_along(keys, "dp", -2)
    down4 = passed_along(down2, "dp", 2)
    up4 = passed_along(up2, "dp", -2)
    sw_own = swapped(keys, "dp")
    sw_down2 = swapped(down2, "dp")
    sw_up2 = swapped(up2, "dp")
    sw_far = swapped(jnp.where(core == 0, up4, down4), "dp")
    key_tiles = [
        ("own", keys, 0),
        ("sw_own", sw_own, delta),
        ("down2", down2, -2),
        ("up2", up2, 2),
        ("sw_down2", sw_down2, delta - 2),
        ("sw_up2", sw_up2, delta + 2),
        ("down4", down4, -4),
        ("up4", up4, 4),
        ("sw_far", sw_far, -3 * delta),
    ]
    run_max = jnp.full((query_rows,), -1e30, jnp.float32)
    run_sum = jnp.zeros((query_rows,), jnp.float32)
    pos_logit = jnp.zeros((query_rows,), jnp.float32)
    stored = []
    for name, key_tile, offset in key_tiles:
        owner_idx = (cycle_index + offset) % cycle_size
        column = lax.dynamic_slice_in_dim(neg_mask, owner_idx, 1, 1)[:, 0]
        hit_block = positive == owner_idx
        allow_block = (column == 1) | hit_block
        allowed = jnp.broadcast_to(
            allow_block[:, None, None], (query_blocks, tile_rows, tile_rows)
        ).reshape(query_rows, tile_rows)
        at_positive = (hit_block[:, None, None] & same_row[None, :, :]).reshape(
            query_rows, tile_rows
        )
        logit_tile = logit_scale * lax.dot_general(
            queries, key_tile, (((1,), (1,)), ((), ())), preferred_element_type=jnp.float32
        )
        masked = jnp.where(allowed, logit_tile, jnp.float32(-1e30))
        next_max = jnp.maximum(run_max, jnp.max(masked, axis=1))
        run_sum = run_sum * jnp.exp(run_max - next_max) + jnp.sum(
            jnp.where(allowed, jnp.exp(masked - next_max[:, None]), 0.0), axis=1
        )
        run_max = next_max
        pos_logit = pos_logit + jnp.sum(jnp.where(at_positive, logit_tile, 0.0), axis=1)
        stored.append((name, key_tile, masked, at_positive))
    log_total = run_max + jnp.log(run_sum)
    row_loss = log_total - pos_logit
    coefficients = []
    for name, key_tile, masked, at_positive in stored:
        softmax_p = jnp.exp(masked - log_total[:, None])
        coefficients.append(
            (row_weight[:, None] * (softmax_p - at_positive.astype(jnp.float32))).astype(jnp.bfloat16)
        )
    order = {name: i for i, (name, _, _, _) in enumerate(stored)}

    def parts_of(names):
        cols = jnp.concatenate([coefficients[order[n]] for n in names], axis=1)
        out = lax.dot_general(
            cols, queries, (((0,), (0,)), ((), ())), preferred_element_type=jnp.float32
        )
        rows = jnp.concatenate([stored[order[n]][1] for n in names], axis=0)
        return {n: out[i * tile_rows : (i + 1) * tile_rows] for i, n in enumerate(names)}, cols, rows

    key_parts, far_cols, far_rows = parts_of(("sw_far", "up4", "down4"))
    near_parts, near_cols, near_rows = parts_of(("own", "sw_own", "down2", "up2", "sw_down2", "sw_up2"))
    key_parts.update(near_parts)
    grad_query = logit_scale * jnp.dot(
        jnp.concatenate([far_cols, near_cols], axis=1),
        jnp.concatenate([far_rows, near_rows], axis=0),
        preferred_element_type=jnp.float32,
    )
    back_own = swapped(key_parts["sw_own"], "dp")
    back_down2 = swapped(key_parts["sw_down2"], "dp")
    back_up2 = swapped(key_parts["sw_up2"], "dp")
    back_far = swapped(key_parts["sw_far"], "dp")
    zero = jnp.zeros_like(back_far)
    far_up = key_parts["up4"] + jnp.where(core == 0, back_far, zero)
    far_down = key_parts["down4"] + jnp.where(core == 0, zero, back_far)
    far_up_in = passed_along(far_up, "dp", 2)
    far_down_in = passed_along(far_down, "dp", -2)
    near_up = key_parts["up2"] + back_up2 + far_up_in
    near_down = key_parts["down2"] + back_down2 + far_down_in
    total = (
        key_parts["own"]
        + back_own
        + passed_along(near_up, "dp", 2)
        + passed_along(near_down, "dp", -2)
    )
    half = tile_rows // 2
    halves = total.reshape(2, half, total.shape[1])
    mine = jnp.where(rep_index == 0, halves[0], halves[1])
    other = jnp.where(rep_index == 0, halves[1], halves[0])
    grad_keys = logit_scale * (mine + lax.ppermute(other, "rep", [(0, 1), (1, 0)]))
    return (row_loss, grad_query, grad_keys)


def solution(mesh):
    placed = (
        P(("dp", "rep"), None),
        P("dp", None),
        P(("dp", "rep"), None),
        P(("dp", "rep")),
        P(("dp", "rep")),
    )
    return jax.shard_map(
        step,
        mesh=mesh,
        in_specs=placed,
        out_specs=(P(("dp", "rep")), P(("dp", "rep"), None), P(("dp", "rep"), None)),
        check_vma=False,
    )
```
